1024 devices in a mesh: slab: 16 (over z_hi, y, core), dp: 64 (over x, z_lo).
Axes of the slice: x: 4, y: 4, z: 32 (z_hi: 2, z_lo: 16; z = z_hi * 16 + z_lo), core: 2. Of those that a mesh axis runs over, the one named last changes fastest.
Arguments:
- inputs: bfloat16 [64, 32, 24, 64, 128], P('dp', 'slab'), may hold values from -6 to 6
- cotangent: bfloat16 [64, 32, 24, 64, 128], P('dp', 'slab'), may hold values from -4 to 4
- spectral_weight: bfloat16 [16, 256, 4096], P('slab', 'dp'), may hold values from -1.5 to 1.5
- w_in: bfloat16 [64, 256], replicated, may hold values from -0.75 to 0.75
- b_in: float32 [256], replicated, may hold values from -3 to 3
- w_out: bfloat16 [256, 64], replicated, may hold values from -0.375 to 0.375
- b_out: float32 [64], replicated, may hold values from -3 to 3
Outputs:
- grad_inputs: bfloat16 [64, 32, 24, 64, 128], P('dp', 'slab')
- grad_spectral: float32 [16, 256, 4096], P('slab', 'dp')
The draws below stay inside these ranges and needn't reach their ends.
All inputs are finite; a program needn't handle non-finite values.
Results may differ from the reference program's by a relative error of at most 0.014.
Values may be sent and summed in bfloat16 or wider, within the bound.
No kernel may reach another device: no remote copies, remote signals or barrier semaphores. Data moves between devices by JAX's collectives and lax.ppermute only.
A program may use at most 32 MiB of HBM per device.

```python
import math
import jax
import jax.numpy as jnp
from jax import lax

C = 64
H = 256
MX = 16
MY = 16
MZ = 16
NX = 32
NY = 24
NZ = 128
BATCH = 64


def shard_levels(stream_key, shape, shards, smallest, top_value):
    level, own = 1.0, jax.random.fold_in(stream_key, 6)
    for dim, blocks in shards:
        steps = jnp.exp(jax.random.uniform(jax.random.fold_in(own, dim), (blocks,), jnp.float32, smallest / len(shards), top_value / len(shards)))
        level = level * jnp.repeat(steps, shape[dim] // blocks).reshape([-1 if axis == dim else 1 for axis in range(len(shape))])
    return level


def gaussian(stream_key, shape, deviation, reach, pieces=(), held_as=jnp.bfloat16):
    drawn = jax.random.normal(stream_key, shape, jnp.float32) * deviation
    if len(pieces) > 0:
        drawn = shard_levels(stream_key, shape, pieces, -0.22, 0.18) * drawn
    return jnp.clip(drawn, min=-reach, max=reach).astype(held_as)


def setup_inputs(seed: int = 0) -> dict:
    splits = jax.random.split(jax.random.key(seed), 8)
    inputs = gaussian(splits[0], (BATCH, NX, NY, C, NZ), 1.0, 6.0, ((0, 64), (1, 16)))
    cotangent = gaussian(splits[1], (BATCH, NX, NY, C, NZ), 0.5, 4.0, ((0, 64), (1, 16)))
    spectral_weight = gaussian(splits[2], (MY, MX * MZ, C * C), (C // 4) ** -0.5, 1.5, ((0, 16), (1, 64)))
    w_in = gaussian(splits[3], (C, H), C ** -0.5, 0.75)
    b_in = gaussian(splits[4], (H,), 0.5, 3.0, (), jnp.float32)
    w_out = gaussian(splits[5], (H, C), H ** -0.5, 0.375)
    b_out = gaussian(splits[6], (C,), 0.5, 3.0, (), jnp.float32)
    return {"inputs": inputs, "cotangent": cotangent, "spectral_weight": spectral_weight, "w_in": w_in, "b_in": b_in, "w_out": w_out, "b_out": b_out}


root_half = 0.7071067811865476
inv_root_two_pi = 0.3989422804014327


def dft_table(length, kept_count):
    half_kept = kept_count // 2
    positions = jnp.arange(length, dtype=jnp.int32)
    cos_freq = jnp.arange(half_kept, dtype=jnp.int32)
    freqs = jnp.concatenate([cos_freq, cos_freq + 1])[:, None]
    phases = ((freqs * positions[None, :]) % length).astype(jnp.float32) * (2.0 * math.pi / length)
    values = jnp.concatenate([jnp.cos(phases[:half_kept]), jnp.sin(phases[half_kept:])], axis=0)
    return values.astype(jnp.bfloat16)


def gelu_value(values_in):
    return 0.5 * values_in * (1.0 + jax.scipy.special.erf(values_in * root_half))


def gelu_slope(values_in):
    return 0.5 * (1.0 + jax.scipy.special.erf(values_in * root_half)) + values_in * jnp.exp(-0.5 * values_in * values_in) * inv_root_two_pi


def fdot(form, left, right):
    return jnp.einsum(form, left.astype(jnp.float32), right.astype(jnp.float32))


def reference(inputs, cotangent, spectral_weight, w_in, b_in, w_out, b_out):
    table_x = dft_table(NX, MX)
    table_y = dft_table(NY, MY)
    table_z = dft_table(NZ, MZ)
    factor = 8.0 / (NX * NY * NZ)
    weights = spectral_weight.reshape(MY, MX, MZ, C, C)

    def analyse(samples):
        along_z = fdot('xycz,kz->xyck', samples, table_z).astype(jnp.bfloat16)
        along_y = fdot('xyck,jy->xjck', along_z, table_y).astype(jnp.bfloat16)
        return fdot('xjck,ix->ijck', along_y, table_x).astype(jnp.bfloat16)

    def synthesise(coeff_in):
        back_x = fdot('ijck,ix->xjck', coeff_in, table_x).astype(jnp.bfloat16)
        back_y = fdot('xjck,jy->xyck', back_x, table_y).astype(jnp.bfloat16)
        return fdot('xyck,kz->xycz', back_y, table_z) * factor

    def one_crop(running, crop_pair):
        samples, upstream = crop_pair
        coeffs = analyse(samples)
        mixed_modes = fdot('ijck,jikco->ijok', coeffs, weights).astype(jnp.bfloat16)
        spectral = synthesise(mixed_modes)
        activation = fdot('xycz,ch->xyhz', samples, w_in) + b_in.astype(jnp.float32)[:, None]
        hidden = gelu_value(activation).astype(jnp.bfloat16)
        pre_gelu = fdot('xyhz,hc->xycz', hidden, w_out) + b_out.astype(jnp.float32)[:, None] + spectral
        grad_pre = (upstream.astype(jnp.float32) * gelu_slope(pre_gelu)).astype(jnp.bfloat16)
        grad_act = (fdot('xycz,hc->xyhz', grad_pre, w_out) * gelu_slope(activation)).astype(jnp.bfloat16)
        grad_coeffs = analyse(grad_pre)
        back_modes = fdot('ijok,jikco->ijck', grad_coeffs, weights).astype(jnp.bfloat16)
        grad_field = (fdot('xyhz,ch->xycz', grad_act, w_in) + synthesise(back_modes)).astype(jnp.bfloat16)
        grad_term = fdot('ijck,ijok->jikco', coeffs, grad_coeffs) * factor
        return running + grad_term, grad_field

    start_sum = jnp.zeros((MY, MX, MZ, C, C), jnp.float32)
    running, grad_inputs = lax.scan(one_crop, start_sum, (inputs, cotangent))
    return grad_inputs, running.reshape(MY, MX * MZ, C * C)
```

```python
import math

import jax
import jax.numpy as jnp
from jax import lax
from jax.sharding import PartitionSpec as P

C = 64
MX = 16
MY = 16
MZ = 16
NX = 32
NY = 24
NZ = 128


root_half = 0.7071067811865476
inv_root_two_pi = 0.3989422804014327


def dft_table(length, kept_count):
    half_kept = kept_count // 2
    positions = jnp.arange(length, dtype=jnp.int32)
    cos_freq = jnp.arange(half_kept, dtype=jnp.int32)
    freqs = jnp.concatenate([cos_freq, cos_freq + 1])[:, None]
    phases = (freqs * positions[None, :] % length).astype(jnp.float32) * (2.0 * math.pi / length)
    values = jnp.concatenate([jnp.cos(phases[:half_kept]), jnp.sin(phases[half_kept:])], axis=0)
    return values.astype(jnp.bfloat16)


def gelu_value(values_in):
    return 0.5 * values_in * (1.0 + jax.scipy.special.erf(values_in * root_half))


def gelu_slope(values_in):
    return (
        0.5 * (1.0 + jax.scipy.special.erf(values_in * root_half))
        + values_in * jnp.exp(-0.5 * values_in * values_in) * inv_root_two_pi
    )


def bdot(form, left, right):
    return jnp.einsum(form, left, right, preferred_element_type=jnp.float32)


def per_device(inputs, cotangent, spectral_weight, w_in, b_in, w_out, b_out):
    slab_count = lax.axis_size("slab")
    group_count = lax.axis_size("dp")
    local_modes = MY // slab_count
    group_modes = MX * MZ // group_count
    crop_count = inputs.shape[0]
    table_x = dft_table(NX, MX)
    table_y = dft_table(NY, MY)
    table_z = dft_table(NZ, MZ)
    factor = 8.0 / (NX * NY * NZ)

    def analyse(samples):
        along_z = bdot("bxycz,kz->bxyck", samples, table_z).astype(jnp.bfloat16)
        along_y = bdot("bxyck,jy->bxjck", along_z, table_y).astype(jnp.bfloat16)
        return bdot(
            "bxjck,ix->bijck",
            lax.all_to_all(along_y, "slab", split_axis=2, concat_axis=1, tiled=True),
            table_x,
        ).astype(jnp.bfloat16)

    def synthesise(coeff_in):
        back_x = bdot("bijck,ix->bxjck", coeff_in, table_x).astype(jnp.bfloat16)
        back_y = bdot(
            "bxjck,jy->bxyck",
            lax.all_to_all(back_x, "slab", split_axis=1, concat_axis=2, tiled=True),
            table_y,
        ).astype(jnp.bfloat16)
        return bdot("bxyck,kz->bxycz", back_y, table_z) * factor

    def send_out(coeff_in):
        ordered = jnp.transpose(coeff_in, (0, 2, 1, 4, 3)).reshape(
            crop_count, local_modes, group_count, group_modes, C
        )
        arrived = lax.all_to_all(ordered, "dp", split_axis=2, concat_axis=0, tiled=True)
        return arrived.reshape(crop_count * group_count, local_modes, group_modes, C)

    def send_back(routed_in):
        returned = lax.all_to_all(
            routed_in.reshape(crop_count * group_count, local_modes, 1, group_modes, C),
            "dp", split_axis=0, concat_axis=2, tiled=True,
        )
        return jnp.transpose(
            returned.reshape(crop_count, local_modes, MX, MZ, C), (0, 2, 1, 4, 3)
        )

    weights = spectral_weight.reshape(local_modes, group_modes, C, C)
    coeffs = analyse(inputs)
    routed = send_out(coeffs)
    mixed_routed = bdot("bjgc,jgco->bjgo", routed, weights).astype(jnp.bfloat16)
    mixed_modes = send_back(mixed_routed)
    spectral = synthesise(mixed_modes)
    activation = bdot("bxycz,ch->bxyhz", inputs, w_in) + b_in[:, None]
    hidden = gelu_value(activation).astype(jnp.bfloat16)
    pre_gelu = bdot("bxyhz,hc->bxycz", hidden, w_out) + b_out[:, None] + spectral
    grad_pre = (cotangent.astype(jnp.float32) * gelu_slope(pre_gelu)).astype(jnp.bfloat16)
    grad_act = (bdot("bxycz,hc->bxyhz", grad_pre, w_out) * gelu_slope(activation)).astype(
        jnp.bfloat16
    )
    grad_coeffs = analyse(grad_pre)
    grad_routed = send_out(grad_coeffs)
    back_routed = bdot("bjgo,jgco->bjgc", grad_routed, weights).astype(jnp.bfloat16)
    back_modes = send_back(back_routed)
    grad_weight = (bdot("bjgc,bjgo->jgco", routed, grad_routed) * factor).reshape(
        local_modes, group_modes, C * C
    )
    grad_field = (bdot("bxyhz,ch->bxycz", grad_act, w_in) + synthesise(back_modes)).astype(
        jnp.bfloat16
    )
    return (grad_field, grad_weight)


def solution(mesh):
    return jax.shard_map(
        per_device,
        mesh=mesh,
        in_specs=(
            P("dp", "slab", None, None, None),
            P("dp", "slab", None, None, None),
            P("slab", "dp", None),
            P(),
            P(),
            P(),
            P(),
        ),
        out_specs=(P("dp", "slab", None, None, None), P("slab", "dp", None)),
        check_vma=False,
    )
```

```python
import math

import jax
import jax.numpy as jnp
from jax import lax
from jax.sharding import Mesh, PartitionSpec as P

C = 64
MX = 16
MY = 16
MZ = 16
NX = 32
NY = 24
NZ = 128


root_half = 0.7071067811865476
inv_root_two_pi = 0.3989422804014327


def dft_table(length, kept_count):
    half_kept = kept_count // 2
    positions = jnp.arange(length, dtype=jnp.int32)
    cos_freq = jnp.arange(half_kept, dtype=jnp.int32)
    freqs = jnp.concatenate([cos_freq, cos_freq + 1])[:, None]
    phases = (freqs * positions[None, :] % length).astype(jnp.float32) * (2.0 * math.pi / length)
    values = jnp.concatenate([jnp.cos(phases[:half_kept]), jnp.sin(phases[half_kept:])], axis=0)
    return values.astype(jnp.bfloat16)


def gelu_value(values_in):
    return 0.5 * values_in * (1.0 + jax.scipy.special.erf(values_in * root_half))


def gelu_slope(values_in):
    return (
        0.5 * (1.0 + jax.scipy.special.erf(values_in * root_half))
        + values_in * jnp.exp(-0.5 * values_in * values_in) * inv_root_two_pi
    )


def bdot(form, left, right):
    return jnp.einsum(form, left, right, preferred_element_type=jnp.float32)


def per_device(inputs, cotangent, spectral_weight, w_in, b_in, w_out, b_out):
    outer_count = lax.axis_size("zh")
    inner_count = lax.axis_size("yc")
    slab_count = outer_count * inner_count
    group_count = lax.axis_size("dp")
    local_modes = MY // slab_count
    group_modes = MX * MZ // group_count
    crop_count = inputs.shape[0]
    table_x = dft_table(NX, MX)
    table_y = dft_table(NY, MY)
    table_z = dft_table(NZ, MZ)
    factor = 8.0 / (NX * NY * NZ)

    def gather_x(local):
        b_, xl, nj, c_, k_ = local.shape
        local = local.reshape(b_, xl, outer_count, inner_count, c_, k_)
        local = jnp.transpose(local, (0, 1, 3, 2, 4, 5)).reshape(b_, xl, nj, c_, k_)
        local = lax.all_to_all(local, "yc", split_axis=2, concat_axis=1, tiled=True)
        return lax.all_to_all(local, "zh", split_axis=2, concat_axis=1, tiled=True)

    def scatter_x(whole):
        whole = lax.all_to_all(whole, "zh", split_axis=1, concat_axis=2, tiled=True)
        whole = lax.all_to_all(whole, "yc", split_axis=1, concat_axis=2, tiled=True)
        b_, xl, nj, c_, k_ = whole.shape
        whole = whole.reshape(b_, xl, inner_count, outer_count, c_, k_)
        return jnp.transpose(whole, (0, 1, 3, 2, 4, 5)).reshape(b_, xl, nj, c_, k_)

    def analyse(samples):
        along_z = bdot("bxycz,kz->bxyck", samples, table_z).astype(jnp.bfloat16)
        along_y = bdot("bxyck,jy->bxjck", along_z, table_y).astype(jnp.bfloat16)
        return bdot("bxjck,ix->bijck", gather_x(along_y), table_x).astype(jnp.bfloat16)

    def synthesise(coeff_in):
        back_x = bdot("bijck,ix->bxjck", coeff_in, table_x).astype(jnp.bfloat16)
        back_y = bdot("bxjck,jy->bxyck", scatter_x(back_x), table_y).astype(jnp.bfloat16)
        return bdot("bxyck,kz->bxycz", back_y, table_z) * factor

    def send_out(coeff_in):
        ordered = jnp.transpose(coeff_in, (0, 2, 1, 4, 3)).reshape(
            crop_count, local_modes, group_count, group_modes, C
        )
        arrived = lax.all_to_all(ordered, "dp", split_axis=2, concat_axis=0, tiled=True)
        return arrived.reshape(crop_count * group_count, local_modes, group_modes, C)

    def send_back(routed_in):
        returned = lax.all_to_all(
            routed_in.reshape(crop_count * group_count, local_modes, 1, group_modes, C),
            "dp", split_axis=0, concat_axis=2, tiled=True,
        )
        return jnp.transpose(
            returned.reshape(crop_count, local_modes, MX, MZ, C), (0, 2, 1, 4, 3)
        )

    weights = spectral_weight.reshape(local_modes, group_modes, C, C)
    coeffs = analyse(inputs)
    routed = send_out(coeffs)
    mixed_routed = bdot("bjgc,jgco->bjgo", routed, weights).astype(jnp.bfloat16)
    mixed_modes = send_back(mixed_routed)
    spectral = synthesise(mixed_modes)
    activation = bdot("bxycz,ch->bxyhz", inputs, w_in) + b_in[:, None]
    hidden = gelu_value(activation).astype(jnp.bfloat16)
    pre_gelu = bdot("bxyhz,hc->bxycz", hidden, w_out) + b_out[:, None] + spectral
    grad_pre = (cotangent.astype(jnp.float32) * gelu_slope(pre_gelu)).astype(jnp.bfloat16)
    grad_act = (bdot("bxycz,hc->bxyhz", grad_pre, w_out) * gelu_slope(activation)).astype(
        jnp.bfloat16
    )
    grad_coeffs = analyse(grad_pre)
    grad_routed = send_out(grad_coeffs)
    back_routed = bdot("bjgo,jgco->bjgc", grad_routed, weights).astype(jnp.bfloat16)
    back_modes = send_back(back_routed)
    grad_weight = (bdot("bjgc,bjgo->jgco", routed, grad_routed) * factor).reshape(
        local_modes, group_modes, C * C
    )
    grad_field = (bdot("bxyhz,ch->bxycz", grad_act, w_in) + synthesise(back_modes)).astype(
        jnp.bfloat16
    )
    return (grad_field, grad_weight)


def solution(mesh):
    slab_size = mesh.shape["slab"]
    inner_size = 8 if slab_size % 8 == 0 else slab_size
    split_mesh = Mesh(
        mesh.devices.reshape(slab_size // inner_size, inner_size, mesh.shape["dp"]),
        ("zh", "yc", "dp"),
    )
    slab = ("zh", "yc")
    return jax.shard_map(
        per_device,
        mesh=split_mesh,
        in_specs=(
            P("dp", slab, None, None, None),
            P("dp", slab, None, None, None),
            P(slab, "dp", None),
            P(),
            P(),
            P(),
            P(),
        ),
        out_specs=(P("dp", slab, None, None, None), P(slab, "dp", None)),
        check_vma=False,
    )
```

```python
import math

import jax
import jax.numpy as jnp
from jax import lax
from jax.sharding import Mesh, PartitionSpec as P

C = 64
MX = 16
MY = 16
MZ = 16
NX = 32
NY = 24
NZ = 128


root_half = 0.7071067811865476
inv_root_two_pi = 0.3989422804014327


def dft_table(length, kept_count):
    half_kept = kept_count // 2
    positions = jnp.arange(length, dtype=jnp.int32)
    cos_freq = jnp.arange(half_kept, dtype=jnp.int32)
    freqs = jnp.concatenate([cos_freq, cos_freq + 1])[:, None]
    phases = (freqs * positions[None, :] % length).astype(jnp.float32) * (2.0 * math.pi / length)
    values = jnp.concatenate([jnp.cos(phases[:half_kept]), jnp.sin(phases[half_kept:])], axis=0)
    return values.astype(jnp.bfloat16)


def gelu_value(values_in):
    return 0.5 * values_in * (1.0 + jax.scipy.special.erf(values_in * root_half))


def gelu_slope(values_in):
    return (
        0.5 * (1.0 + jax.scipy.special.erf(values_in * root_half))
        + values_in * jnp.exp(-0.5 * values_in * values_in) * inv_root_two_pi
    )


def bdot(form, left, right):
    return jnp.einsum(form, left, right, preferred_element_type=jnp.float32)


def per_device(inputs, cotangent, spectral_weight, w_in, b_in, w_out, b_out):
    outer_count = lax.axis_size("zh")
    inner_count = lax.axis_size("yc")
    slab_count = outer_count * inner_count
    group_count = lax.axis_size("dp")
    local_modes = MY // slab_count
    group_modes = MX * MZ // group_count
    crop_count = inputs.shape[0]
    table_x = dft_table(NX, MX)
    table_y = dft_table(NY, MY)
    table_z = dft_table(NZ, MZ)
    factor = 8.0 / (NX * NY * NZ)

    def gather_inner(local):
        b_, xl, nj, c_, k_ = local.shape
        local = local.reshape(b_, xl, outer_count, inner_count, c_, k_)
        local = jnp.transpose(local, (0, 1, 3, 2, 4, 5)).reshape(b_, xl, nj, c_, k_)
        return lax.all_to_all(local, "yc", split_axis=2, concat_axis=1, tiled=True)

    def scatter_inner(whole):
        whole = lax.all_to_all(whole, "yc", split_axis=1, concat_axis=2, tiled=True)
        b_, xl, nj, c_, k_ = whole.shape
        whole = whole.reshape(b_, xl, inner_count, outer_count, c_, k_)
        return jnp.transpose(whole, (0, 1, 3, 2, 4, 5)).reshape(b_, xl, nj, c_, k_)

    half_cells = NX // outer_count
    table_half = lax.dynamic_slice_in_dim(
        table_x, lax.axis_index("zh") * half_cells, half_cells, axis=1
    )
    owners = ("zh", "dp")

    def analyse(samples):
        along_z = bdot("bxycz,kz->bxyck", samples, table_z).astype(jnp.bfloat16)
        along_y = bdot("bxyck,jy->bxjck", along_z, table_y).astype(jnp.bfloat16)
        partial = bdot("bxjck,ix->jbikc", gather_inner(along_y), table_half)
        ordered = partial.reshape(outer_count, crop_count, group_count, group_modes, C)
        ordered = jnp.transpose(ordered, (0, 2, 1, 3, 4)).reshape(
            outer_count * group_count * crop_count, group_modes, C
        )
        arrived = lax.all_to_all(ordered, owners, split_axis=0, concat_axis=0, tiled=True)
        summed = arrived.reshape(outer_count, group_count * crop_count, group_modes, C).sum(0)
        return summed.astype(jnp.bfloat16).reshape(
            group_count * crop_count, local_modes, group_modes, C
        )

    def synthesise(routed_in):
        sent = jnp.broadcast_to(
            routed_in.reshape(1, group_count * crop_count, group_modes, C),
            (outer_count, group_count * crop_count, group_modes, C),
        ).reshape(outer_count * group_count * crop_count, group_modes, C)
        arrived = lax.all_to_all(sent, owners, split_axis=0, concat_axis=0, tiled=True)
        arrived = jnp.transpose(
            arrived.reshape(outer_count, group_count, crop_count, group_modes, C), (2, 0, 1, 3, 4)
        ).reshape(crop_count, outer_count, MX, MZ, C)
        back_x = bdot("bjiko,ix->bxjok", arrived, table_half).astype(jnp.bfloat16)
        back_y = bdot("bxjck,jy->bxyck", scatter_inner(back_x), table_y).astype(jnp.bfloat16)
        return bdot("bxyck,kz->bxycz", back_y, table_z) * factor

    weights = spectral_weight.reshape(local_modes, group_modes, C, C)
    routed = analyse(inputs)
    mixed_routed = bdot("bjgc,jgco->bjgo", routed, weights).astype(jnp.bfloat16)
    spectral = synthesise(mixed_routed)
    activation = bdot("bxycz,ch->bxyhz", inputs, w_in) + b_in[:, None]
    hidden = gelu_value(activation).astype(jnp.bfloat16)
    pre_gelu = bdot("bxyhz,hc->bxycz", hidden, w_out) + b_out[:, None] + spectral
    grad_pre = (cotangent.astype(jnp.float32) * gelu_slope(pre_gelu)).astype(jnp.bfloat16)
    grad_act = (bdot("bxycz,hc->bxyhz", grad_pre, w_out) * gelu_slope(activation)).astype(
        jnp.bfloat16
    )
    grad_routed = analyse(grad_pre)
    back_routed = bdot("bjgo,jgco->bjgc", grad_routed, weights).astype(jnp.bfloat16)
    grad_weight = (bdot("bjgc,bjgo->jgco", routed, grad_routed) * factor).reshape(
        local_modes, group_modes, C * C
    )
    grad_field = (bdot("bxyhz,ch->bxycz", grad_act, w_in) + synthesise(back_routed)).astype(
        jnp.bfloat16
    )
    return (grad_field, grad_weight)


def solution(mesh):
    slab_size = mesh.shape["slab"]
    inner_size = 8 if slab_size % 8 == 0 else slab_size
    split_mesh = Mesh(
        mesh.devices.reshape(slab_size // inner_size, inner_size, mesh.shape["dp"]),
        ("zh", "yc", "dp"),
    )
    slab = ("zh", "yc")
    return jax.shard_map(
        per_device,
        mesh=split_mesh,
        in_specs=(
            P("dp", slab, None, None, None),
            P("dp", slab, None, None, None),
            P(slab, "dp", None),
            P(),
            P(),
            P(),
            P(),
        ),
        out_specs=(P("dp", slab, None, None, None), P(slab, "dp", None)),
        check_vma=False,
    )
```

```python
import math

import jax
import jax.numpy as jnp
from jax import lax
from jax.sharding import Mesh, PartitionSpec as P

C = 64
MX = 16
MY = 16
MZ = 16
NX = 32
NY = 24
NZ = 128


root_half = 0.7071067811865476
inv_root_two_pi = 0.3989422804014327


def dft_table(length, kept_count):
    half_kept = kept_count // 2
    positions = jnp.arange(length, dtype=jnp.int32)
    cos_freq = jnp.arange(half_kept, dtype=jnp.int32)
    freqs = jnp.concatenate([cos_freq, cos_freq + 1])[:, None]
    phases = (freqs * positions[None, :] % length).astype(jnp.float32) * (2.0 * math.pi / length)
    values = jnp.concatenate([jnp.cos(phases[:half_kept]), jnp.sin(phases[half_kept:])], axis=0)
    return values.astype(jnp.bfloat16)


def gelu_value(values_in):
    return 0.5 * values_in * (1.0 + jax.scipy.special.erf(values_in * root_half))


def gelu_slope(values_in):
    return (
        0.5 * (1.0 + jax.scipy.special.erf(values_in * root_half))
        + values_in * jnp.exp(-0.5 * values_in * values_in) * inv_root_two_pi
    )


def bdot(form, left, right):
    return jnp.einsum(form, left, right, preferred_element_type=jnp.float32)


def per_device(inputs, cotangent, spectral_weight, w_in, b_in, w_out, b_out):
    outer_count = lax.axis_size("zh")
    inner_count = lax.axis_size("yc")
    slab_count = outer_count * inner_count
    group_count = lax.axis_size("dp")
    local_modes = MY // slab_count
    group_modes = MX * MZ // group_count
    crop_count = inputs.shape[0]
    table_x = dft_table(NX, MX)
    table_y = dft_table(NY, MY)
    table_z = dft_table(NZ, MZ)
    factor = 8.0 / (NX * NY * NZ)

    def gather_inner(local):
        b_, xl, nj, c_, k_ = local.shape
        local = local.reshape(b_, xl, outer_count, inner_count, c_, k_)
        local = jnp.transpose(local, (0, 1, 3, 2, 4, 5)).reshape(b_, xl, nj, c_, k_)
        return lax.all_to_all(local, "yc", split_axis=2, concat_axis=1, tiled=True)

    def scatter_inner(whole):
        whole = lax.all_to_all(whole, "yc", split_axis=1, concat_axis=2, tiled=True)
        b_, xl, nj, c_, k_ = whole.shape
        whole = whole.reshape(b_, xl, inner_count, outer_count, c_, k_)
        return jnp.transpose(whole, (0, 1, 3, 2, 4, 5)).reshape(b_, xl, nj, c_, k_)

    half_cells = NX // outer_count
    table_half = lax.dynamic_slice_in_dim(
        table_x, lax.axis_index("zh") * half_cells, half_cells, axis=1
    )
    owners = ("zh", "dp")

    def analyse(samples):
        along_z = bdot("bxycz,kz->bxyck", samples, table_z).astype(jnp.bfloat16)
        along_y = bdot("bxyck,jy->bxjck", along_z, table_y).astype(jnp.bfloat16)
        partial = bdot("bxjck,ix->jbikc", gather_inner(along_y), table_half)
        ordered = partial.reshape(outer_count, crop_count, group_count, group_modes, C)
        ordered = jnp.transpose(ordered, (0, 2, 1, 3, 4)).reshape(
            outer_count * group_count * crop_count, group_modes, C
        ).astype(jnp.bfloat16)
        arrived = lax.all_to_all(ordered, owners, split_axis=0, concat_axis=0, tiled=True)
        summed = arrived.astype(jnp.float32).reshape(
            outer_count, group_count * crop_count, group_modes, C
        ).sum(0)
        return summed.astype(jnp.bfloat16).reshape(
            group_count * crop_count, local_modes, group_modes, C
        )

    def synthesise(routed_in):
        sent = jnp.broadcast_to(
            routed_in.reshape(1, group_count * crop_count, group_modes, C),
            (outer_count, group_count * crop_count, group_modes, C),
        ).reshape(outer_count * group_count * crop_count, group_modes, C)
        arrived = lax.all_to_all(sent, owners, split_axis=0, concat_axis=0, tiled=True)
        arrived = jnp.transpose(
            arrived.reshape(outer_count, group_count, crop_count, group_modes, C), (2, 0, 1, 3, 4)
        ).reshape(crop_count, outer_count, MX, MZ, C)
        back_x = bdot("bjiko,ix->bxjok", arrived, table_half).astype(jnp.bfloat16)
        back_y = bdot("bxjck,jy->bxyck", scatter_inner(back_x), table_y).astype(jnp.bfloat16)
        return bdot("bxyck,kz->bxycz", back_y, table_z) * factor

    weights = spectral_weight.reshape(local_modes, group_modes, C, C)
    routed = analyse(inputs)
    mixed_routed = bdot("bjgc,jgco->bjgo", routed, weights).astype(jnp.bfloat16)
    spectral = synthesise(mixed_routed)
    activation = bdot("bxycz,ch->bxyhz", inputs, w_in) + b_in[:, None]
    hidden = gelu_value(activation).astype(jnp.bfloat16)
    pre_gelu = bdot("bxyhz,hc->bxycz", hidden, w_out) + b_out[:, None] + spectral
    grad_pre = (cotangent.astype(jnp.float32) * gelu_slope(pre_gelu)).astype(jnp.bfloat16)
    grad_act = (bdot("bxycz,hc->bxyhz", grad_pre, w_out) * gelu_slope(activation)).astype(
        jnp.bfloat16
    )
    grad_routed = analyse(grad_pre)
    back_routed = bdot("bjgo,jgco->bjgc", grad_routed, weights).astype(jnp.bfloat16)
    grad_weight = (bdot("bjgc,bjgo->jgco", routed, grad_routed) * factor).reshape(
        local_modes, group_modes, C * C
    )
    grad_field = (bdot("bxyhz,ch->bxycz", grad_act, w_in) + synthesise(back_routed)).astype(
        jnp.bfloat16
    )
    return (grad_field, grad_weight)


def solution(mesh):
    slab_size = mesh.shape["slab"]
    inner_size = 8 if slab_size % 8 == 0 else slab_size
    split_mesh = Mesh(
        mesh.devices.reshape(slab_size // inner_size, inner_size, mesh.shape["dp"]),
        ("zh", "yc", "dp"),
    )
    slab = ("zh", "yc")
    return jax.shard_map(
        per_device,
        mesh=split_mesh,
        in_specs=(
            P("dp", slab, None, None, None),
            P("dp", slab, None, None, None),
            P(slab, "dp", None),
            P(),
            P(),
            P(),
            P(),
        ),
        out_specs=(P("dp", slab, None, None, None), P(slab, "dp", None)),
        check_vma=False,
    )
```

```python
import math

import jax
import jax.numpy as jnp
from jax import lax
from jax.sharding import Mesh, PartitionSpec as P

C = 64
MX = 16
MY = 16
MZ = 16
NX = 32
NY = 24
NZ = 128


root_half = 0.7071067811865476
inv_root_two_pi = 0.3989422804014327


def dft_table(length, kept_count):
    half_kept = kept_count // 2
    positions = jnp.arange(length, dtype=jnp.int32)
    cos_freq = jnp.arange(half_kept, dtype=jnp.int32)
    freqs = jnp.concatenate([cos_freq, cos_freq + 1])[:, None]
    phases = (freqs * positions[None, :] % length).astype(jnp.float32) * (2.0 * math.pi / length)
    values = jnp.concatenate([jnp.cos(phases[:half_kept]), jnp.sin(phases[half_kept:])], axis=0)
    return values.astype(jnp.bfloat16)


def gelu_value(values_in):
    return 0.5 * values_in * (1.0 + jax.scipy.special.erf(values_in * root_half))


def gelu_slope(values_in):
    return (
        0.5 * (1.0 + jax.scipy.special.erf(values_in * root_half))
        + values_in * jnp.exp(-0.5 * values_in * values_in) * inv_root_two_pi
    )


def bdot(form, left, right):
    return jnp.einsum(form, left, right, preferred_element_type=jnp.float32)


def per_device(inputs, cotangent, spectral_weight, w_in, b_in, w_out, b_out):
    outer_count = lax.axis_size("zh")
    inner_count = lax.axis_size("yc")
    slab_count = outer_count * inner_count
    group_count = lax.axis_size("dp")
    local_modes = MY // slab_count
    group_modes = MX * MZ // group_count
    crop_count = inputs.shape[0]
    table_x = dft_table(NX, MX)
    table_y = dft_table(NY, MY)
    table_z = dft_table(NZ, MZ)
    factor = 8.0 / (NX * NY * NZ)

    def gather_inner(local):
        b_, xl, nj, c_, k_ = local.shape
        local = local.reshape(b_, xl, outer_count, inner_count, c_, k_)
        local = jnp.transpose(local, (0, 1, 3, 2, 4, 5)).reshape(b_, xl, nj, c_, k_)
        return lax.all_to_all(local, "yc", split_axis=2, concat_axis=1, tiled=True)

    def scatter_inner(whole):
        whole = lax.all_to_all(whole, "yc", split_axis=1, concat_axis=2, tiled=True)
        b_, xl, nj, c_, k_ = whole.shape
        whole = whole.reshape(b_, xl, inner_count, outer_count, c_, k_)
        return jnp.transpose(whole, (0, 1, 3, 2, 4, 5)).reshape(b_, xl, nj, c_, k_)

    half_cells = NX // outer_count
    table_half = lax.dynamic_slice_in_dim(
        table_x, lax.axis_index("zh") * half_cells, half_cells, axis=1
    )
    owners = ("zh", "dp")

    def analyse(samples):
        along_z = bdot("bxycz,kz->bxyck", samples, table_z).astype(jnp.bfloat16)
        along_y = bdot("bxyck,jy->bxjck", along_z, table_y).astype(jnp.bfloat16)
        partial = bdot("bxjck,ix->jbikc", gather_inner(along_y), table_half)
        ordered = partial.reshape(outer_count, crop_count, group_count, group_modes, C)
        ordered = jnp.transpose(ordered, (0, 2, 1, 3, 4)).reshape(
            outer_count * group_count * crop_count, group_modes, C
        ).astype(jnp.bfloat16)
        arrived = lax.all_to_all(ordered, owners, split_axis=0, concat_axis=0, tiled=True)
        summed = arrived.astype(jnp.float32).reshape(
            outer_count, group_count * crop_count, group_modes, C
        ).sum(0)
        return summed.astype(jnp.bfloat16).reshape(
            group_count * crop_count, local_modes, group_modes, C
        )

    def synthesise(routed_in):
        sent = jnp.broadcast_to(
            routed_in.reshape(1, group_count * crop_count, group_modes, C),
            (outer_count, group_count * crop_count, group_modes, C),
        ).reshape(outer_count * group_count * crop_count, group_modes, C)
        arrived = lax.all_to_all(sent, owners, split_axis=0, concat_axis=0, tiled=True)
        arrived = jnp.transpose(
            arrived.reshape(outer_count, group_count, crop_count, group_modes, C), (2, 0, 1, 3, 4)
        ).reshape(crop_count, outer_count, MX, MZ, C)
        back_x = bdot("bjiko,ix->bxjok", arrived, table_half).astype(jnp.bfloat16)
        back_y = bdot("bxjck,jy->bxyck", scatter_inner(back_x), table_y).astype(jnp.bfloat16)
        return bdot("bxyck,kz->bxycz", back_y, table_z) * factor

    weights = spectral_weight.reshape(local_modes, group_modes, C, C)
    routed = analyse(inputs)
    mixed_routed = bdot("bjgc,jgco->bjgo", routed, weights).astype(jnp.bfloat16)
    spectral = synthesise(mixed_routed)
    activation = bdot("bxycz,ch->bxyhz", inputs, w_in) + b_in[:, None]
    hidden = gelu_value(activation).astype(jnp.bfloat16)
    channel_out, activation = lax.optimization_barrier(
        (bdot("bxyhz,hc->bxycz", hidden, w_out) + b_out[:, None], activation)
    )
    pre_gelu = channel_out + spectral
    grad_pre = (cotangent.astype(jnp.float32) * gelu_slope(pre_gelu)).astype(jnp.bfloat16)
    grad_act = (bdot("bxycz,hc->bxyhz", grad_pre, w_out) * gelu_slope(activation)).astype(
        jnp.bfloat16
    )
    grad_routed = analyse(grad_pre)
    back_routed = bdot("bjgo,jgco->bjgc", grad_routed, weights).astype(jnp.bfloat16)
    grad_weight = (bdot("bjgc,bjgo->jgco", routed, grad_routed) * factor).reshape(
        local_modes, group_modes, C * C
    )
    grad_field = (bdot("bxyhz,ch->bxycz", grad_act, w_in) + synthesise(back_routed)).astype(
        jnp.bfloat16
    )
    return (grad_field, grad_weight)


def solution(mesh):
    slab_size = mesh.shape["slab"]
    inner_size = 8 if slab_size % 8 == 0 else slab_size
    split_mesh = Mesh(
        mesh.devices.reshape(slab_size // inner_size, inner_size, mesh.shape["dp"]),
        ("zh", "yc", "dp"),
    )
    slab = ("zh", "yc")
    return jax.shard_map(
        per_device,
        mesh=split_mesh,
        in_specs=(
            P("dp", slab, None, None, None),
            P("dp", slab, None, None, None),
            P(slab, "dp", None),
            P(),
            P(),
            P(),
            P(),
        ),
        out_specs=(P("dp", slab, None, None, None), P(slab, "dp", None)),
        check_vma=False,
    )
```

```python
import math

import jax
import jax.numpy as jnp
from jax import lax
from jax.sharding import Mesh, PartitionSpec as P

C = 64
MX = 16
MY = 16
MZ = 16
NX = 32
NY = 24
NZ = 128


root_half = 0.7071067811865476
inv_root_two_pi = 0.3989422804014327


def dft_table(length, kept_count):
    half_kept = kept_count // 2
    positions = jnp.arange(length, dtype=jnp.int32)
    cos_freq = jnp.arange(half_kept, dtype=jnp.int32)
    freqs = jnp.concatenate([cos_freq, cos_freq + 1])[:, None]
    phases = (freqs * positions[None, :] % length).astype(jnp.float32) * (2.0 * math.pi / length)
    values = jnp.concatenate([jnp.cos(phases[:half_kept]), jnp.sin(phases[half_kept:])], axis=0)
    return values.astype(jnp.bfloat16)


def gelu_value(values_in):
    return 0.5 * values_in * (1.0 + jax.scipy.special.erf(values_in * root_half))


def gelu_slope(values_in):
    return (
        0.5 * (1.0 + jax.scipy.special.erf(values_in * root_half))
        + values_in * jnp.exp(-0.5 * values_in * values_in) * inv_root_two_pi
    )


def bdot(form, left, right):
    return jnp.einsum(form, left, right, preferred_element_type=jnp.float32)


def per_device(inputs, cotangent, spectral_weight, w_in, b_in, w_out, b_out):
    outer_count = lax.axis_size("zh")
    inner_count = lax.axis_size("yc")
    slab_count = outer_count * inner_count
    group_count = lax.axis_size("dp")
    local_modes = MY // slab_count
    group_modes = MX * MZ // group_count
    crop_count = inputs.shape[0]
    table_x = dft_table(NX, MX)
    table_y = dft_table(NY, MY)
    table_z = dft_table(NZ, MZ)
    factor = 8.0 / (NX * NY * NZ)

    def gather_inner(local):
        b_, xl, nj, c_, k_ = local.shape
        local = local.reshape(b_, xl, outer_count, inner_count, c_, k_)
        local = jnp.transpose(local, (0, 1, 3, 2, 4, 5)).reshape(b_, xl, nj, c_, k_)
        return lax.all_to_all(local, "yc", split_axis=2, concat_axis=1, tiled=True)

    def scatter_inner(whole):
        whole = lax.all_to_all(whole, "yc", split_axis=1, concat_axis=2, tiled=True)
        b_, xl, nj, c_, k_ = whole.shape
        whole = whole.reshape(b_, xl, inner_count, outer_count, c_, k_)
        return jnp.transpose(whole, (0, 1, 3, 2, 4, 5)).reshape(b_, xl, nj, c_, k_)

    half_cells = NX // outer_count
    table_half = lax.dynamic_slice_in_dim(
        table_x, lax.axis_index("zh") * half_cells, half_cells, axis=1
    )
    owners = ("zh", "dp")

    def analyse(samples):
        along_z = bdot("bxycz,kz->bxyck", samples, table_z).astype(jnp.bfloat16)
        along_y = bdot("bxyck,jy->bxjck", along_z, table_y).astype(jnp.bfloat16)
        partial = bdot("bxjck,ix->jbikc", gather_inner(along_y), table_half)
        ordered = partial.reshape(outer_count, crop_count, group_count, group_modes, C)
        ordered = jnp.transpose(ordered, (0, 2, 1, 3, 4)).reshape(
            outer_count * group_count * crop_count, group_modes, C
        ).astype(jnp.bfloat16)
        arrived = lax.all_to_all(ordered, owners, split_axis=0, concat_axis=0, tiled=True)
        summed = arrived.astype(jnp.float32).reshape(
            outer_count, group_count * crop_count, group_modes, C
        ).sum(0)
        return summed.astype(jnp.bfloat16).reshape(
            group_count * crop_count, local_modes, group_modes, C
        )

    def synthesise(routed_in):
        sent = jnp.broadcast_to(
            routed_in.reshape(1, group_count * crop_count, group_modes, C),
            (outer_count, group_count * crop_count, group_modes, C),
        ).reshape(outer_count * group_count * crop_count, group_modes, C)
        arrived = lax.all_to_all(sent, owners, split_axis=0, concat_axis=0, tiled=True)
        arrived = jnp.transpose(
            arrived.reshape(outer_count, group_count, crop_count, group_modes, C), (2, 0, 1, 3, 4)
        ).reshape(crop_count, outer_count, MX, MZ, C)
        back_x = bdot("bjiko,ix->bxjok", arrived, table_half).astype(jnp.bfloat16)
        back_y = bdot("bxjck,jy->bxyck", scatter_inner(back_x), table_y).astype(jnp.bfloat16)
        return bdot("bxyck,kz->bxycz", back_y, table_z) * factor

    weights = spectral_weight.reshape(local_modes, group_modes, C, C)
    routed = analyse(inputs)
    mixed_routed = bdot("bjgc,jgco->bjgo", routed, weights).astype(jnp.bfloat16)
    spectral = synthesise(mixed_routed)
    activation = bdot("bxycz,ch->bxyhz", inputs, w_in) + b_in[:, None]
    hidden = gelu_value(activation).astype(jnp.bfloat16)
    channel_out, activation = lax.optimization_barrier(
        (bdot("bxyhz,hc->bxycz", hidden, w_out) + b_out[:, None], activation)
    )
    pre_gelu = channel_out + spectral
    grad_pre = (cotangent.astype(jnp.float32) * gelu_slope(pre_gelu)).astype(jnp.bfloat16)
    grad_act = (bdot("bxycz,hc->bxyhz", grad_pre, w_out) * gelu_slope(activation)).astype(
        jnp.bfloat16
    )
    grad_routed = analyse(grad_pre)
    back_routed = bdot("bjgo,jgco->bjgc", grad_routed, weights).astype(jnp.bfloat16)
    grad_weight = (bdot("bjgc,bjgo->jgco", routed, grad_routed) * factor).reshape(
        local_modes, group_modes, C * C
    )
    channel_grad = lax.optimization_barrier(bdot("bxyhz,ch->bxycz", grad_act, w_in))
    grad_field = (channel_grad + synthesise(back_routed)).astype(jnp.bfloat16)
    return (grad_field, grad_weight)


def solution(mesh):
    slab_size = mesh.shape["slab"]
    inner_size = 8 if slab_size % 8 == 0 else slab_size
    split_mesh = Mesh(
        mesh.devices.reshape(slab_size // inner_size, inner_size, mesh.shape["dp"]),
        ("zh", "yc", "dp"),
    )
    slab = ("zh", "yc")
    return jax.shard_map(
        per_device,
        mesh=split_mesh,
        in_specs=(
            P("dp", slab, None, None, None),
            P("dp", slab, None, None, None),
            P(slab, "dp", None),
            P(),
            P(),
            P(),
            P(),
        ),
        out_specs=(P("dp", slab, None, None, None), P(slab, "dp", None)),
        check_vma=False,
    )
```
